1024 devices in a mesh: section: 32 (over y, x_lo, core), mp: 16 (over z), dp: 2 (over x_hi).
Axes of the slice: x: 4 (x_hi: 2, x_lo: 2; x = x_hi * 2 + x_lo), y: 8, z: 16, core: 2. Of those that a mesh axis runs over, the one named last changes fastest.
Arguments:
- lower_out: bfloat16 [32, 2, 256, 3072], P('section', 'dp', None, 'mp'), may hold values from -6 to 6
- upper_out: bfloat16 [32, 2, 256, 3072], P('section', 'dp', None, 'mp'), may hold values from -40 to 40
- lower_grad: bfloat16 [32, 2, 256, 3072], P('section', 'dp', None, 'mp'), may hold values from -1.5 to 1.5
- upper_grad: bfloat16 [32, 2, 256, 3072], P('section', 'dp', None, 'mp'), may hold values from -6 to 6
- norm_gain: bfloat16 [32, 3072], P('section'), may hold values from 0.5 to 1.5
- query_weight: bfloat16 [32, 3072, 4096], P('section', None, 'mp'), may hold values from -1 to 1
- key_weight: bfloat16 [32, 3072, 2048], P('section', None, 'mp'), may hold values from -2 to 2
- value_projection: bfloat16 [32, 3072, 2048], P('section', None, 'mp'), may hold values from -0.109375 to 0.109375
- output_weight: bfloat16 [32, 4096, 3072], P('section', 'mp'), may hold values from -0.375 to 0.375
- key_lists: int32 [2, 2], replicated, may hold values from -1 to 1, as said below
Outputs:
- rebuilt_lower: bfloat16 [32, 2, 256, 3072], P('section', 'dp', None, 'mp')
- upper_in_grad: bfloat16 [32, 2, 256, 3072], P('section', 'dp', None, 'mp')
- gain_grad: float32 [32, 3072], P('section', 'mp')
The draws below stay inside these ranges and needn't reach their ends.
Inputs may be any that keep to these rules, and one draw needn't show every extreme that they name: `key_lists`: row r names the key blocks that query block r attends to, in increasing order, then -1 in the remaining entries; every row names its own block; exactly one row names all 2 blocks, and every other row names exactly 1 block, its own.
All inputs are finite; a program needn't handle non-finite values.
Results may differ from the reference program's by a relative error of at most 0.024.
The reference program's roundings to bfloat16 on the way count: a program that leaves them out, or rounds other values in their place, can miss the bound.
Values may be sent and summed in bfloat16 or wider, within the bound.
No kernel may reach another device: no remote copies, remote signals or barrier semaphores. Data moves between devices by JAX's collectives and lax.ppermute only.
A program may use at most 64 MiB of HBM per device.

```python
import math
import jax
import jax.numpy as jnp
from jax import lax

STREAM_FEATURES = 3072
QUERY_HEADS = 32
KEY_VALUE_HEADS = 16
HEAD_SIZE = 128
BLOCK = 128
TOKEN_COUNT = 256
LAYER_COUNT = 32
SEQS = 2
N_MP = 16


def weight_pair(key):
    query_row_block = jax.random.truncated_normal(jax.random.fold_in(key, 41), -4.0, 4.0, (LAYER_COUNT, STREAM_FEATURES, QUERY_HEADS * HEAD_SIZE), jnp.float32) / math.sqrt(STREAM_FEATURES)
    key_row_block = jax.random.truncated_normal(jax.random.fold_in(key, 42), -4.0, 4.0, (LAYER_COUNT, STREAM_FEATURES, KEY_VALUE_HEADS * HEAD_SIZE), jnp.float32) / math.sqrt(STREAM_FEATURES)
    return (query_row_block, key_row_block)


def draw_query_weight(key, part):
    query_row_block, key_row_block = weight_pair(key)
    return jnp.clip(query_row_block, -1.0, 1.0).astype(jnp.bfloat16)


def draw_key_weight(key, part):
    query_row_block, key_row_block = weight_pair(key)
    return key_row_block.astype(jnp.bfloat16)


def draw_upper_out(key, part):
    return jax.random.truncated_normal(jax.random.fold_in(key, 35), -6.0, 6.0, (LAYER_COUNT, SEQS, TOKEN_COUNT, STREAM_FEATURES), jnp.float32).astype(jnp.bfloat16)


def draw_key_lists(key, part):
    blocks = TOKEN_COUNT // BLOCK
    rows = jnp.arange(blocks, dtype=jnp.int32)
    limit = max(1, blocks // 2)
    priority = jax.random.randint(jax.random.fold_in(key, 21), (blocks, blocks), 0, 1 << 20, jnp.int32)
    priority = priority * blocks + rows[None, :]
    diagonal = rows[:, None] == rows[None, :]
    priority = jnp.where(diagonal, -1, priority)
    rank = jnp.sum((priority[:, None, :] < priority[:, :, None]).astype(jnp.int32), axis=2)
    chosen = (rank < limit).astype(jnp.int32)
    full_row = jax.random.randint(jax.random.fold_in(key, 22), (), 0, blocks, jnp.int32)
    chosen = jnp.where((rows == full_row)[:, None], 1, chosen)
    ranking = (1 - chosen) * blocks + rows[None, :]
    ordering = jnp.argsort(ranking, axis=1, stable=True).astype(jnp.int32)
    picked = jnp.take_along_axis(chosen, ordering, axis=1)
    return jnp.where(picked == 1, ordering, -1).astype(jnp.int32)


def block_levels(rng, shape, cuts, least, largest):
    def one(position, shards_of):
        steps = jax.random.uniform(jax.random.fold_in(jax.random.fold_in(rng, 6), position), (shards_of,), jnp.float32, least / len(cuts), largest / len(cuts))
        return jnp.repeat(jnp.exp(steps), shape[position] // shards_of).reshape((-1,) + (1,) * (len(shape) - position - 1))

    factor_of = one(*cuts[0])
    for cut in cuts[1:]:
        factor_of = factor_of * one(*cut)
    return factor_of


def gaussian(rng, extent, scale, most, split=(), held_as=jnp.bfloat16):
    values = jax.random.normal(rng, extent, jnp.float32) * scale
    if len(split) > 0:
        values = block_levels(rng, extent, split, -0.22, 0.18) * values
    return jnp.clip(values, min=-most, max=most).astype(held_as)


def setup_inputs(seed: int = 0) -> dict:
    arg_keys = jax.random.split(jax.random.key(seed), 11)
    lower_out = gaussian(arg_keys[0], (LAYER_COUNT, SEQS, TOKEN_COUNT, STREAM_FEATURES), 1.0, 6.0, ((0, 32), (1, 2), (3, 16)))
    upper_out = draw_upper_out(jax.random.fold_in(arg_keys[10], 71), 0)
    lower_grad = gaussian(arg_keys[2], (LAYER_COUNT, SEQS, TOKEN_COUNT, STREAM_FEATURES), 0.25, 1.5, ((0, 32), (1, 2), (3, 16)))
    upper_grad = gaussian(arg_keys[3], (LAYER_COUNT, SEQS, TOKEN_COUNT, STREAM_FEATURES), 1.0, 6.0, ((0, 32), (1, 2), (3, 16)))
    norm_gain = jnp.clip(1.0 + 0.1 * jax.random.normal(arg_keys[4], (LAYER_COUNT, STREAM_FEATURES), jnp.float32), 0.5, 1.5).astype(jnp.bfloat16)
    query_weight = draw_query_weight(jax.random.fold_in(arg_keys[10], 71), 0)
    key_weight = draw_key_weight(jax.random.fold_in(arg_keys[10], 71), 0)
    value_projection = gaussian(arg_keys[7], (LAYER_COUNT, STREAM_FEATURES, KEY_VALUE_HEADS * HEAD_SIZE), STREAM_FEATURES ** -0.5, 0.109375, ((0, 32), (2, 16)))
    output_weight = gaussian(arg_keys[8], (LAYER_COUNT, QUERY_HEADS * HEAD_SIZE, STREAM_FEATURES), (QUERY_HEADS * HEAD_SIZE // 16) ** -0.5, 0.375, ((0, 32), (1, 16)))
    key_lists = draw_key_lists(jax.random.fold_in(arg_keys[10], 71), 0)
    return dict(lower_out=lower_out, upper_out=upper_out, lower_grad=lower_grad, upper_grad=upper_grad, norm_gain=norm_gain, query_weight=query_weight, key_weight=key_weight, value_projection=value_projection, output_weight=output_weight, key_lists=key_lists)


def token_mask(key_lists):
    blocks = key_lists.shape[0]
    columns = jnp.arange(blocks, dtype=jnp.int32)
    block_table = jnp.any(key_lists[:, :, None] == columns[None, None, :], axis=1)
    return jnp.repeat(jnp.repeat(block_table, BLOCK, axis=0), BLOCK, axis=1)

def layer_backward(lower_out, upper_out, lower_grad, upper_grad, gain_row, w_query, w_key, w_value, w_output, allowed):
    stream = upper_out.astype(jnp.float32)
    inverse = lax.rsqrt(lax.optimization_barrier(jnp.mean(stream * stream, axis=1, keepdims=True)) + 1e-06)
    unit_rows = stream * inverse
    gain_rows = gain_row.astype(jnp.float32)
    normed = (unit_rows * gain_rows).astype(jnp.bfloat16)
    group_width = QUERY_HEADS // KEY_VALUE_HEADS
    query_matrix = jnp.dot(normed, w_query, preferred_element_type=jnp.float32).astype(jnp.bfloat16)
    key_matrix = jnp.dot(normed, w_key, preferred_element_type=jnp.float32).astype(jnp.bfloat16)
    value_matrix = jnp.dot(normed, w_value, preferred_element_type=jnp.float32).astype(jnp.bfloat16)
    query_head_split = query_matrix.astype(jnp.float32).reshape(TOKEN_COUNT, KEY_VALUE_HEADS, group_width, HEAD_SIZE)
    key_head_split = key_matrix.astype(jnp.float32).reshape(TOKEN_COUNT, KEY_VALUE_HEADS, HEAD_SIZE)
    value_head_split = value_matrix.astype(jnp.float32).reshape(TOKEN_COUNT, KEY_VALUE_HEADS, HEAD_SIZE)
    raw_scores = jnp.einsum('qjgd,kjd->jgqk', query_head_split, key_head_split) / math.sqrt(HEAD_SIZE)
    masked = jnp.where(allowed, raw_scores, -1e+30)
    row_max = lax.optimization_barrier(jnp.max(masked, axis=3, keepdims=True))
    exponent = jnp.where(allowed, jnp.exp(masked - row_max), 0.0)
    row_total = lax.optimization_barrier(jnp.sum(exponent, axis=3, keepdims=True))
    probs_full = exponent / row_total
    probability_half = probs_full.astype(jnp.bfloat16)
    attended = jnp.einsum('jgqk,kjd->qjgd', probability_half.astype(jnp.float32), value_head_split)
    attended = attended.astype(jnp.bfloat16).reshape(TOKEN_COUNT, QUERY_HEADS * HEAD_SIZE)
    shard_cols = QUERY_HEADS * HEAD_SIZE // N_MP
    parts = jnp.einsum('lmc,mce->mle', attended.astype(jnp.float32).reshape(TOKEN_COUNT, N_MP, shard_cols), w_output.astype(jnp.float32).reshape(N_MP, shard_cols, STREAM_FEATURES))
    parts_half = lax.optimization_barrier(parts.astype(jnp.bfloat16))
    out_sum = lax.optimization_barrier(jnp.sum(parts_half.astype(jnp.float32), axis=0))
    rebuilt = (lower_out.astype(jnp.float32) - out_sum).astype(jnp.bfloat16)
    attention_gradient = jnp.dot(lower_grad, w_output.T, preferred_element_type=jnp.float32).astype(jnp.bfloat16)
    attention_gradient = attention_gradient.astype(jnp.float32).reshape(TOKEN_COUNT, KEY_VALUE_HEADS, group_width, HEAD_SIZE)
    prob_grad = jnp.einsum('qjgd,kjd->jgqk', attention_gradient, value_head_split)
    score_gradient = probs_full * (prob_grad - lax.optimization_barrier(jnp.sum(prob_grad * probs_full, axis=3, keepdims=True))) / math.sqrt(HEAD_SIZE)
    score_gradient = score_gradient.astype(jnp.bfloat16).astype(jnp.float32)
    value_gradient = jnp.einsum('munr,nmuy->rmy', probability_half.astype(jnp.float32), attention_gradient).astype(jnp.bfloat16).reshape(TOKEN_COUNT, KEY_VALUE_HEADS * HEAD_SIZE)
    query_grad = jnp.einsum('jgqk,kjd->qjgd', score_gradient, key_head_split).astype(jnp.bfloat16).reshape(TOKEN_COUNT, QUERY_HEADS * HEAD_SIZE)
    key_gradient = jnp.einsum('munr,nmuy->rmy', score_gradient, query_head_split).astype(jnp.bfloat16).reshape(TOKEN_COUNT, KEY_VALUE_HEADS * HEAD_SIZE)
    normed_grad = jnp.dot(query_grad, w_query.T, preferred_element_type=jnp.float32)
    normed_grad = normed_grad + jnp.dot(key_gradient, w_key.T, preferred_element_type=jnp.float32)
    normed_grad = normed_grad + jnp.dot(value_gradient, w_value.T, preferred_element_type=jnp.float32)
    weighted = gain_rows * normed_grad
    row_stat = lax.optimization_barrier(jnp.mean(unit_rows * weighted, axis=1, keepdims=True))
    entering = (upper_grad.astype(jnp.float32) + (weighted - unit_rows * row_stat) * inverse).astype(jnp.bfloat16)
    gain_part = lax.optimization_barrier(jnp.sum(normed_grad * unit_rows, axis=0))
    return (rebuilt, entering, gain_part)

def reference(lower_out, upper_out, lower_grad, upper_grad, norm_gain, query_weight, key_weight, value_projection, output_weight, key_lists):
    allowed = token_mask(key_lists)

    def per_section(items):
        lower_s, upper_s, lgrad_s, ugrad_s, gain_s, wq_s, wk_s, wv_s, wo_s = items
        rebuilt_list = []
        entering_list = []
        gain_total = jnp.zeros((STREAM_FEATURES,), jnp.float32)
        for member in range(SEQS):
            rebuilt, entering, gain_part = layer_backward(lower_s[member], upper_s[member], lgrad_s[member], ugrad_s[member], gain_s, wq_s, wk_s, wv_s, wo_s, allowed)
            rebuilt_list.append(rebuilt)
            entering_list.append(entering)
            gain_total = gain_total + gain_part
        return (jnp.stack(rebuilt_list), jnp.stack(entering_list), gain_total)
    rebuilt_all, entering_all, gain_grad = lax.map(per_section, (lower_out, upper_out, lower_grad, upper_grad, norm_gain, query_weight, key_weight, value_projection, output_weight))
    rebuilt_lower = jnp.concatenate([rebuilt_all[1:], jnp.zeros_like(rebuilt_all[:1])], axis=0)
    upper_in_grad = jnp.concatenate([entering_all[1:], jnp.zeros_like(entering_all[:1])], axis=0)
    return (rebuilt_lower, upper_in_grad, gain_grad)
```

```python
import math

import jax
import jax.numpy as jnp
from jax import lax
from jax.sharding import PartitionSpec as P

HEAD_SIZE = 128


def from_behind(x, axis, by):
    length = lax.axis_size(axis)
    pairs = [(i, i + by) for i in range(length) if 0 <= i + by < length]
    return lax.ppermute(x, axis, pairs)


def shift(x, axis, by):
    length = lax.axis_size(axis)
    return lax.ppermute(x, axis, [(i, (i + by) % length) for i in range(length)])


def ring_gather(chunk, axis):
    n = lax.axis_size(axis)
    me = lax.axis_index(axis)
    forward_steps = n // 2
    backward_steps = n - 1 - forward_steps
    relative = [None] * n
    relative[0] = chunk
    forward = chunk
    backward = chunk
    for step in range(forward_steps):
        forward = shift(forward, axis, 1)
        relative[n - 1 - step] = forward
        if step < backward_steps:
            backward = shift(backward, axis, -1)
            relative[step + 1] = backward
    stacked = jnp.stack(relative)
    return jnp.roll(stacked, me, axis=0)


def ring_reduce_scatter(parts, axis, extra=None):
    n = lax.axis_size(axis)
    me = lax.axis_index(axis)
    forward_steps = n // 2
    backward_steps = n - 1 - forward_steps

    def pick(stack, offset):
        return lax.dynamic_index_in_dim(stack, (me + offset) % n, 0, keepdims=False)

    def part_at(offset):
        head = pick(parts, offset).astype(jnp.float32)
        if extra is None:
            return (head,)
        return (head, pick(extra, offset))

    def wire(values):
        return (values[0].astype(jnp.bfloat16),) + tuple(values[1:])

    def add(received, offset):
        own = part_at(offset)
        return tuple(r.astype(jnp.float32) + o for r, o in zip(received, own))

    forward = wire(part_at(forward_steps))
    backward = wire(part_at(n - backward_steps))
    for step in range(forward_steps):
        forward = shift(forward, axis, 1)
        if step < forward_steps - 1:
            forward = wire(add(forward, forward_steps - 1 - step))
        if step < backward_steps:
            backward = shift(backward, axis, -1)
            if step < backward_steps - 1:
                backward = wire(add(backward, n - backward_steps + 1 + step))
    own = part_at(0)
    return tuple(
        o + f.astype(jnp.float32) + b.astype(jnp.float32) for o, f, b in zip(own, forward, backward)
    )


def token_mask(key_lists, length):
    blocks = key_lists.shape[0]
    columns = jnp.arange(blocks, dtype=jnp.int32)
    block_table = jnp.any(key_lists[:, :, None] == columns[None, None, :], axis=1).astype(
        jnp.float32
    )
    owner = (jnp.arange(length, dtype=jnp.int32) // (length // blocks))[:, None] == columns[None, :]
    one_hot = owner.astype(jnp.float32)
    return jnp.dot(jnp.dot(one_hot, block_table), one_hot.T) > 0.5


def local(
    lower_out,
    upper_out,
    lower_grad,
    upper_grad,
    norm_gain,
    query_weight,
    key_weight,
    value_projection,
    output_weight,
    key_lists,
):
    n_mp = lax.axis_size("mp")
    share = upper_out.shape[3]
    gathered = ring_gather(jnp.stack([upper_out[0, 0], lower_grad[0, 0]]), "mp")
    length = gathered.shape[2]
    whole_upper = jnp.transpose(gathered[:, 0], (1, 0, 2)).reshape(length, n_mp * share)
    whole_grad = jnp.transpose(gathered[:, 1], (1, 0, 2)).reshape(length, n_mp * share)
    stream = whole_upper.astype(jnp.float32)
    inverse = lax.rsqrt(jnp.mean(stream * stream, axis=1, keepdims=True) + 1e-06)
    unit_rows = stream * inverse
    gain_rows = norm_gain[0].astype(jnp.float32)
    normed = (unit_rows * gain_rows).astype(jnp.bfloat16)
    w_query = query_weight[0]
    w_key = key_weight[0]
    w_value = value_projection[0]
    w_output = output_weight[0]
    kv_heads = w_key.shape[1] // HEAD_SIZE
    group_width = w_query.shape[1] // HEAD_SIZE // kv_heads
    query_head_split = jnp.dot(normed, w_query, preferred_element_type=jnp.float32).astype(
        jnp.bfloat16
    )
    query_head_split = query_head_split.reshape(length, kv_heads, group_width, HEAD_SIZE)
    key_head_split = (
        jnp.dot(normed, w_key, preferred_element_type=jnp.float32)
        .astype(jnp.bfloat16)
        .reshape(length, kv_heads, HEAD_SIZE)
    )
    value_head_split = (
        jnp.dot(normed, w_value, preferred_element_type=jnp.float32)
        .astype(jnp.bfloat16)
        .reshape(length, kv_heads, HEAD_SIZE)
    )
    allowed = token_mask(key_lists, length)
    raw_scores = jnp.einsum(
        "qjgd,kjd->jgqk", query_head_split, key_head_split, preferred_element_type=jnp.float32
    ) / math.sqrt(HEAD_SIZE)
    masked = jnp.where(allowed, raw_scores, -1e30)
    row_max = jnp.max(masked, axis=3, keepdims=True)
    exponent = jnp.where(allowed, jnp.exp(masked - row_max), 0.0)
    row_total = jnp.sum(exponent, axis=3, keepdims=True)
    probs_full = exponent / row_total
    probability_half = probs_full.astype(jnp.bfloat16)
    attended = jnp.einsum(
        "jgqk,kjd->qjgd", probability_half, value_head_split, preferred_element_type=jnp.float32
    )
    attended = attended.astype(jnp.bfloat16).reshape(length, -1)
    out_parts = jnp.einsum(
        "lc,cmf->mlf",
        attended,
        w_output.reshape(w_output.shape[0], n_mp, share),
        preferred_element_type=jnp.float32,
    ).astype(jnp.bfloat16)
    (out_share,) = ring_reduce_scatter(out_parts, "mp")
    rebuilt = (lower_out[0, 0].astype(jnp.float32) - out_share).astype(jnp.bfloat16)
    attention_gradient = jnp.dot(whole_grad, w_output.T, preferred_element_type=jnp.float32).astype(
        jnp.bfloat16
    )
    attention_gradient = attention_gradient.reshape(length, kv_heads, group_width, HEAD_SIZE)
    prob_grad = jnp.einsum(
        "qjgd,kjd->jgqk", attention_gradient, value_head_split, preferred_element_type=jnp.float32
    )
    score_gradient = (
        probs_full
        * (prob_grad - jnp.sum(prob_grad * probs_full, axis=3, keepdims=True))
        / math.sqrt(HEAD_SIZE)
    )
    score_gradient = score_gradient.astype(jnp.bfloat16)
    value_gradient = jnp.einsum(
        "munr,nmuy->rmy", probability_half, attention_gradient, preferred_element_type=jnp.float32
    )
    value_gradient = value_gradient.astype(jnp.bfloat16).reshape(length, -1)
    query_grad = jnp.einsum(
        "jgqk,kjd->qjgd", score_gradient, key_head_split, preferred_element_type=jnp.float32
    )
    query_grad = query_grad.astype(jnp.bfloat16).reshape(length, -1)
    key_gradient = jnp.einsum(
        "munr,nmuy->rmy", score_gradient, query_head_split, preferred_element_type=jnp.float32
    )
    key_gradient = key_gradient.astype(jnp.bfloat16).reshape(length, -1)
    normed_grad = jnp.dot(query_grad, w_query.T, preferred_element_type=jnp.float32)
    normed_grad = normed_grad + jnp.dot(key_gradient, w_key.T, preferred_element_type=jnp.float32)
    normed_grad = normed_grad + jnp.dot(
        value_gradient, w_value.T, preferred_element_type=jnp.float32
    )
    weighted = gain_rows * normed_grad
    row_stat = jnp.mean(unit_rows * weighted, axis=1, keepdims=True)
    grad_parts = ((weighted - unit_rows * row_stat) * inverse).astype(jnp.bfloat16)
    grad_parts = jnp.transpose(grad_parts.reshape(length, n_mp, share), (1, 0, 2))
    gain_parts = jnp.sum(normed_grad * unit_rows, axis=0).reshape(n_mp, share)
    grad_share, gain_share = ring_reduce_scatter(grad_parts, "mp", gain_parts)
    lower_rows = upper_grad[0, 0].astype(jnp.float32) + grad_share
    gain_grad = gain_share + shift(gain_share, "dp", 1)
    entering = lower_rows.astype(jnp.bfloat16)
    sent_lower, sent_grad = from_behind((rebuilt, entering), "section", -1)
    return (sent_lower[None, None], sent_grad[None, None], gain_grad[None])


def solution(mesh):
    placed = (
        P("section", "dp", None, "mp"),
        P("section", "dp", None, "mp"),
        P("section", "dp", None, "mp"),
        P("section", "dp", None, "mp"),
        P("section", None),
        P("section", None, "mp"),
        P("section", None, "mp"),
        P("section", None, "mp"),
        P("section", "mp", None),
        P(),
    )
    return jax.shard_map(
        local,
        mesh=mesh,
        in_specs=placed,
        out_specs=(
            P("section", "dp", None, "mp"),
            P("section", "dp", None, "mp"),
            P("section", "mp"),
        ),
        check_vma=False,
    )
```

```python
import math

import jax
import jax.numpy as jnp
from jax import lax
from jax.sharding import PartitionSpec as P

HEAD_SIZE = 128


def from_behind(x, axis, by):
    length = lax.axis_size(axis)
    pairs = [(i, i + by) for i in range(length) if 0 <= i + by < length]
    return lax.ppermute(x, axis, pairs)


def shift(x, axis, by):
    length = lax.axis_size(axis)
    return lax.ppermute(x, axis, [(i, (i + by) % length) for i in range(length)])


def ring_gather(chunk, axis):
    n = lax.axis_size(axis)
    me = lax.axis_index(axis)
    forward_steps = n // 2
    backward_steps = n - 1 - forward_steps
    relative = [None] * n
    relative[0] = chunk
    forward = chunk
    backward = chunk
    for step in range(forward_steps):
        forward = shift(forward, axis, 1)
        relative[n - 1 - step] = forward
        if step < backward_steps:
            backward = shift(backward, axis, -1)
            relative[step + 1] = backward
    stacked = jnp.stack(relative)
    return jnp.roll(stacked, me, axis=0)


def ring_reduce_scatter(parts, exact, axis):
    n = lax.axis_size(axis)
    me = lax.axis_index(axis)
    rows, columns = parts.shape[1], parts.shape[2]
    pad = 16 - 2
    forward_steps = n // 2
    backward_steps = n - 1 - forward_steps

    def pick(stack, offset):
        return lax.dynamic_index_in_dim(stack, (me + offset) % n, 0, keepdims=False)

    def own(offset):
        return pick(parts, offset).astype(jnp.float32), pick(exact, offset)

    def wire(values):
        main, extra = values
        high = extra.astype(jnp.bfloat16)
        low = (extra - high.astype(jnp.float32)).astype(jnp.bfloat16)
        return jnp.concatenate(
            [main.astype(jnp.bfloat16), high[None], low[None], jnp.zeros((pad, columns), jnp.bfloat16)]
        )

    def unwire(packet):
        main = packet[:rows].astype(jnp.float32)
        extra = packet[rows].astype(jnp.float32) + packet[rows + 1].astype(jnp.float32)
        return main, extra

    def add(packet, offset):
        main, extra = unwire(packet)
        own_main, own_extra = own(offset)
        return main + own_main, extra + own_extra

    forward = wire(own(forward_steps))
    backward = wire(own(n - backward_steps))
    for step in range(forward_steps):
        forward = shift(forward, axis, 1)
        if step < forward_steps - 1:
            forward = wire(add(forward, forward_steps - 1 - step))
        if step < backward_steps:
            backward = shift(backward, axis, -1)
            if step < backward_steps - 1:
                backward = wire(add(backward, n - backward_steps + 1 + step))
    own_main, own_extra = own(0)
    forward_main, forward_extra = unwire(forward)
    backward_main, backward_extra = unwire(backward)
    return own_main + forward_main + backward_main, own_extra + forward_extra + backward_extra


def token_mask(key_lists, length):
    blocks = key_lists.shape[0]
    columns = jnp.arange(blocks, dtype=jnp.int32)
    block_table = jnp.any(key_lists[:, :, None] == columns[None, None, :], axis=1).astype(
        jnp.float32
    )
    owner = (jnp.arange(length, dtype=jnp.int32) // (length // blocks))[:, None] == columns[None, :]
    one_hot = owner.astype(jnp.float32)
    return jnp.dot(jnp.dot(one_hot, block_table), one_hot.T) > 0.5


def local(
    lower_out,
    upper_out,
    lower_grad,
    upper_grad,
    norm_gain,
    query_weight,
    key_weight,
    value_projection,
    output_weight,
    key_lists,
):
    n_mp = lax.axis_size("mp")
    share = upper_out.shape[3]
    gathered = ring_gather(jnp.stack([upper_out[0, 0], lower_grad[0, 0]]), "mp")
    length = gathered.shape[2]
    whole_upper = jnp.transpose(gathered[:, 0], (1, 0, 2)).reshape(length, n_mp * share)
    whole_grad = jnp.transpose(gathered[:, 1], (1, 0, 2)).reshape(length, n_mp * share)
    stream = whole_upper.astype(jnp.float32)
    inverse = lax.rsqrt(jnp.mean(stream * stream, axis=1, keepdims=True) + 1e-06)
    unit_rows = stream * inverse
    gain_rows = norm_gain[0].astype(jnp.float32)
    normed = (unit_rows * gain_rows).astype(jnp.bfloat16)
    w_query = query_weight[0]
    w_key = key_weight[0]
    w_value = value_projection[0]
    w_output = output_weight[0]
    kv_heads = w_key.shape[1] // HEAD_SIZE
    group_width = w_query.shape[1] // HEAD_SIZE // kv_heads
    query_head_split = jnp.dot(normed, w_query, preferred_element_type=jnp.float32).astype(
        jnp.bfloat16
    )
    query_head_split = query_head_split.reshape(length, kv_heads, group_width, HEAD_SIZE)
    key_head_split = (
        jnp.dot(normed, w_key, preferred_element_type=jnp.float32)
        .astype(jnp.bfloat16)
        .reshape(length, kv_heads, HEAD_SIZE)
    )
    value_head_split = (
        jnp.dot(normed, w_value, preferred_element_type=jnp.float32)
        .astype(jnp.bfloat16)
        .reshape(length, kv_heads, HEAD_SIZE)
    )
    allowed = token_mask(key_lists, length)
    raw_scores = jnp.einsum(
        "qjgd,kjd->jgqk", query_head_split, key_head_split, preferred_element_type=jnp.float32
    ) / math.sqrt(HEAD_SIZE)
    masked = jnp.where(allowed, raw_scores, -1e30)
    row_max = jnp.max(masked, axis=3, keepdims=True)
    exponent = jnp.where(allowed, jnp.exp(masked - row_max), 0.0)
    row_total = jnp.sum(exponent, axis=3, keepdims=True)
    probs_full = exponent / row_total
    probability_half = probs_full.astype(jnp.bfloat16)
    attended = jnp.einsum(
        "jgqk,kjd->qjgd", probability_half, value_head_split, preferred_element_type=jnp.float32
    )
    attended = attended.astype(jnp.bfloat16).reshape(length, -1)
    out_parts = jnp.einsum(
        "lc,cmf->mlf",
        attended,
        w_output.reshape(w_output.shape[0], n_mp, share),
        preferred_element_type=jnp.float32,
    ).astype(jnp.bfloat16)
    attention_gradient = jnp.dot(whole_grad, w_output.T, preferred_element_type=jnp.float32).astype(
        jnp.bfloat16
    )
    attention_gradient = attention_gradient.reshape(length, kv_heads, group_width, HEAD_SIZE)
    prob_grad = jnp.einsum(
        "qjgd,kjd->jgqk", attention_gradient, value_head_split, preferred_element_type=jnp.float32
    )
    score_gradient = (
        probs_full
        * (prob_grad - jnp.sum(prob_grad * probs_full, axis=3, keepdims=True))
        / math.sqrt(HEAD_SIZE)
    )
    score_gradient = score_gradient.astype(jnp.bfloat16)
    value_gradient = jnp.einsum(
        "munr,nmuy->rmy", probability_half, attention_gradient, preferred_element_type=jnp.float32
    )
    value_gradient = value_gradient.astype(jnp.bfloat16).reshape(length, -1)
    query_grad = jnp.einsum(
        "jgqk,kjd->qjgd", score_gradient, key_head_split, preferred_element_type=jnp.float32
    )
    query_grad = query_grad.astype(jnp.bfloat16).reshape(length, -1)
    key_gradient = jnp.einsum(
        "munr,nmuy->rmy", score_gradient, query_head_split, preferred_element_type=jnp.float32
    )
    key_gradient = key_gradient.astype(jnp.bfloat16).reshape(length, -1)
    normed_grad = jnp.dot(query_grad, w_query.T, preferred_element_type=jnp.float32)
    normed_grad = normed_grad + jnp.dot(key_gradient, w_key.T, preferred_element_type=jnp.float32)
    normed_grad = normed_grad + jnp.dot(
        value_gradient, w_value.T, preferred_element_type=jnp.float32
    )
    weighted = gain_rows * normed_grad
    row_stat = jnp.mean(unit_rows * weighted, axis=1, keepdims=True)
    grad_parts = ((weighted - unit_rows * row_stat) * inverse).astype(jnp.bfloat16)
    grad_parts = jnp.transpose(grad_parts.reshape(length, n_mp, share), (1, 0, 2))
    gain_parts = jnp.sum(normed_grad * unit_rows, axis=0).reshape(n_mp, share)
    shares, gain_share = ring_reduce_scatter(
        jnp.concatenate([out_parts, grad_parts], axis=1), gain_parts, "mp"
    )
    out_share, grad_share = shares[:length], shares[length:]
    rebuilt = (lower_out[0, 0].astype(jnp.float32) - out_share).astype(jnp.bfloat16)
    lower_rows = upper_grad[0, 0].astype(jnp.float32) + grad_share
    gain_grad = gain_share + shift(gain_share, "dp", 1)
    entering = lower_rows.astype(jnp.bfloat16)
    sent = from_behind(jnp.stack([rebuilt, entering]), "section", -1)
    return (sent[0][None, None], sent[1][None, None], gain_grad[None])


def solution(mesh):
    placed = (
        P("section", "dp", None, "mp"),
        P("section", "dp", None, "mp"),
        P("section", "dp", None, "mp"),
        P("section", "dp", None, "mp"),
        P("section", None),
        P("section", None, "mp"),
        P("section", None, "mp"),
        P("section", None, "mp"),
        P("section", "mp", None),
        P(),
    )
    return jax.shard_map(
        local,
        mesh=mesh,
        in_specs=placed,
        out_specs=(
            P("section", "dp", None, "mp"),
            P("section", "dp", None, "mp"),
            P("section", "mp"),
        ),
        check_vma=False,
    )
```

```python
import math

import jax
import jax.numpy as jnp
from jax import lax
from jax.sharding import PartitionSpec as P

HEAD_SIZE = 128


def from_behind(x, axis, by):
    length = lax.axis_size(axis)
    pairs = [(i, i + by) for i in range(length) if 0 <= i + by < length]
    return lax.ppermute(x, axis, pairs)


def shift(x, axis, by):
    length = lax.axis_size(axis)
    return lax.ppermute(x, axis, [(i, (i + by) % length) for i in range(length)])


def ring_gather(chunk, axis):
    n = lax.axis_size(axis)
    me = lax.axis_index(axis)
    forward_steps = n // 2
    backward_steps = n - 1 - forward_steps
    relative = [None] * n
    relative[0] = chunk
    forward = chunk
    backward = chunk
    for step in range(forward_steps):
        forward = shift(forward, axis, 1)
        relative[n - 1 - step] = forward
        if step < backward_steps:
            backward = shift(backward, axis, -1)
            relative[step + 1] = backward
    stacked = jnp.stack(relative)
    return jnp.roll(stacked, me, axis=0)


def ring_reduce_scatter(parts, exact, axis):
    n = lax.axis_size(axis)
    me = lax.axis_index(axis)
    rows, columns = parts.shape[1], parts.shape[2]
    pad = 16 - 2
    forward_steps = n // 2
    backward_steps = n - 1 - forward_steps

    def pick(stack, offset):
        return lax.dynamic_index_in_dim(stack, (me + offset) % n, 0, keepdims=False)

    def own(offset):
        return pick(parts, offset).astype(jnp.float32), pick(exact, offset)

    def wire(values):
        main, extra = values
        high = extra.astype(jnp.bfloat16)
        low = (extra - high.astype(jnp.float32)).astype(jnp.bfloat16)
        return jnp.concatenate(
            [main.astype(jnp.bfloat16), high[None], low[None], jnp.zeros((pad, columns), jnp.bfloat16)]
        )

    def unwire(packet):
        main = packet[:rows].astype(jnp.float32)
        extra = packet[rows].astype(jnp.float32) + packet[rows + 1].astype(jnp.float32)
        return main, extra

    def add(packet, offset):
        main, extra = unwire(packet)
        own_main, own_extra = own(offset)
        return main + own_main, extra + own_extra

    forward = wire(own(forward_steps))
    backward = wire(own(n - backward_steps))
    for step in range(forward_steps):
        forward = shift(forward, axis, 1)
        if step < backward_steps:
            backward = shift(backward, axis, -1)
            forward, backward = lax.optimization_barrier((forward, backward))
            if step < backward_steps - 1:
                backward = wire(add(backward, n - backward_steps + 1 + step))
        if step < forward_steps - 1:
            forward = wire(add(forward, forward_steps - 1 - step))
    own_main, own_extra = own(0)
    forward_main, forward_extra = unwire(forward)
    backward_main, backward_extra = unwire(backward)
    return own_main + forward_main + backward_main, own_extra + forward_extra + backward_extra


def token_mask(key_lists, length):
    blocks = key_lists.shape[0]
    columns = jnp.arange(blocks, dtype=jnp.int32)
    block_table = jnp.any(key_lists[:, :, None] == columns[None, None, :], axis=1).astype(
        jnp.float32
    )
    owner = (jnp.arange(length, dtype=jnp.int32) // (length // blocks))[:, None] == columns[None, :]
    one_hot = owner.astype(jnp.float32)
    return jnp.dot(jnp.dot(one_hot, block_table), one_hot.T) > 0.5


def local(
    lower_out,
    upper_out,
    lower_grad,
    upper_grad,
    norm_gain,
    query_weight,
    key_weight,
    value_projection,
    output_weight,
    key_lists,
):
    n_mp = lax.axis_size("mp")
    share = upper_out.shape[3]
    gathered = ring_gather(jnp.stack([upper_out[0, 0], lower_grad[0, 0]]), "mp")
    length = gathered.shape[2]
    whole_upper = jnp.transpose(gathered[:, 0], (1, 0, 2)).reshape(length, n_mp * share)
    whole_grad = jnp.transpose(gathered[:, 1], (1, 0, 2)).reshape(length, n_mp * share)
    stream = whole_upper.astype(jnp.float32)
    inverse = lax.rsqrt(jnp.mean(stream * stream, axis=1, keepdims=True) + 1e-06)
    unit_rows = stream * inverse
    gain_rows = norm_gain[0].astype(jnp.float32)
    normed = (unit_rows * gain_rows).astype(jnp.bfloat16)
    w_query = query_weight[0]
    w_key = key_weight[0]
    w_value = value_projection[0]
    w_output = output_weight[0]
    kv_heads = w_key.shape[1] // HEAD_SIZE
    group_width = w_query.shape[1] // HEAD_SIZE // kv_heads
    query_head_split = jnp.dot(normed, w_query, preferred_element_type=jnp.float32).astype(
        jnp.bfloat16
    )
    query_head_split = query_head_split.reshape(length, kv_heads, group_width, HEAD_SIZE)
    key_head_split = (
        jnp.dot(normed, w_key, preferred_element_type=jnp.float32)
        .astype(jnp.bfloat16)
        .reshape(length, kv_heads, HEAD_SIZE)
    )
    value_head_split = (
        jnp.dot(normed, w_value, preferred_element_type=jnp.float32)
        .astype(jnp.bfloat16)
        .reshape(length, kv_heads, HEAD_SIZE)
    )
    allowed = token_mask(key_lists, length)
    raw_scores = jnp.einsum(
        "qjgd,kjd->jgqk", query_head_split, key_head_split, preferred_element_type=jnp.float32
    ) / math.sqrt(HEAD_SIZE)
    masked = jnp.where(allowed, raw_scores, -1e30)
    row_max = jnp.max(masked, axis=3, keepdims=True)
    exponent = jnp.where(allowed, jnp.exp(masked - row_max), 0.0)
    row_total = jnp.sum(exponent, axis=3, keepdims=True)
    probs_full = exponent / row_total
    probability_half = probs_full.astype(jnp.bfloat16)
    attended = jnp.einsum(
        "jgqk,kjd->qjgd", probability_half, value_head_split, preferred_element_type=jnp.float32
    )
    attended = attended.astype(jnp.bfloat16).reshape(length, -1)
    out_parts = jnp.einsum(
        "lc,cmf->mlf",
        attended,
        w_output.reshape(w_output.shape[0], n_mp, share),
        preferred_element_type=jnp.float32,
    ).astype(jnp.bfloat16)
    attention_gradient = jnp.dot(whole_grad, w_output.T, preferred_element_type=jnp.float32).astype(
        jnp.bfloat16
    )
    attention_gradient = attention_gradient.reshape(length, kv_heads, group_width, HEAD_SIZE)
    prob_grad = jnp.einsum(
        "qjgd,kjd->jgqk", attention_gradient, value_head_split, preferred_element_type=jnp.float32
    )
    score_gradient = (
        probs_full
        * (prob_grad - jnp.sum(prob_grad * probs_full, axis=3, keepdims=True))
        / math.sqrt(HEAD_SIZE)
    )
    score_gradient = score_gradient.astype(jnp.bfloat16)
    value_gradient = jnp.einsum(
        "munr,nmuy->rmy", probability_half, attention_gradient, preferred_element_type=jnp.float32
    )
    value_gradient = value_gradient.astype(jnp.bfloat16).reshape(length, -1)
    query_grad = jnp.einsum(
        "jgqk,kjd->qjgd", score_gradient, key_head_split, preferred_element_type=jnp.float32
    )
    query_grad = query_grad.astype(jnp.bfloat16).reshape(length, -1)
    key_gradient = jnp.einsum(
        "munr,nmuy->rmy", score_gradient, query_head_split, preferred_element_type=jnp.float32
    )
    key_gradient = key_gradient.astype(jnp.bfloat16).reshape(length, -1)
    normed_grad = jnp.dot(query_grad, w_query.T, preferred_element_type=jnp.float32)
    normed_grad = normed_grad + jnp.dot(key_gradient, w_key.T, preferred_element_type=jnp.float32)
    normed_grad = normed_grad + jnp.dot(
        value_gradient, w_value.T, preferred_element_type=jnp.float32
    )
    weighted = gain_rows * normed_grad
    row_stat = jnp.mean(unit_rows * weighted, axis=1, keepdims=True)
    grad_parts = ((weighted - unit_rows * row_stat) * inverse).astype(jnp.bfloat16)
    grad_parts = jnp.transpose(grad_parts.reshape(length, n_mp, share), (1, 0, 2))
    gain_parts = jnp.sum(normed_grad * unit_rows, axis=0).reshape(n_mp, share)
    shares, gain_share = ring_reduce_scatter(
        jnp.concatenate([out_parts, grad_parts], axis=1), gain_parts, "mp"
    )
    out_share, grad_share = shares[:length], shares[length:]
    rebuilt = (lower_out[0, 0].astype(jnp.float32) - out_share).astype(jnp.bfloat16)
    lower_rows = upper_grad[0, 0].astype(jnp.float32) + grad_share
    gain_grad = gain_share + shift(gain_share, "dp", 1)
    entering = lower_rows.astype(jnp.bfloat16)
    sent = from_behind(jnp.stack([rebuilt, entering]), "section", -1)
    return (sent[0][None, None], sent[1][None, None], gain_grad[None])


def solution(mesh):
    placed = (
        P("section", "dp", None, "mp"),
        P("section", "dp", None, "mp"),
        P("section", "dp", None, "mp"),
        P("section", "dp", None, "mp"),
        P("section", None),
        P("section", None, "mp"),
        P("section", None, "mp"),
        P("section", None, "mp"),
        P("section", "mp", None),
        P(),
    )
    return jax.shard_map(
        local,
        mesh=mesh,
        in_specs=placed,
        out_specs=(
            P("section", "dp", None, "mp"),
            P("section", "dp", None, "mp"),
            P("section", "mp"),
        ),
        check_vma=False,
    )
```

```python
import math

import jax
import jax.numpy as jnp
from jax import lax
from jax.sharding import PartitionSpec as P

HEAD_SIZE = 128


def from_behind(x, axis, by):
    length = lax.axis_size(axis)
    pairs = [(i, i + by) for i in range(length) if 0 <= i + by < length]
    return lax.ppermute(x, axis, pairs)


def shift(x, axis, by):
    length = lax.axis_size(axis)
    return lax.ppermute(x, axis, [(i, (i + by) % length) for i in range(length)])


def ring_gather(chunk, axis):
    n = lax.axis_size(axis)
    me = lax.axis_index(axis)
    forward_steps = n // 2
    backward_steps = n - 1 - forward_steps
    relative = [None] * n
    relative[0] = chunk
    forward = chunk
    backward = chunk
    for step in range(forward_steps):
        forward = shift(forward, axis, 1)
        relative[n - 1 - step] = forward
        if step < backward_steps:
            backward = shift(backward, axis, -1)
            relative[step + 1] = backward
    stacked = jnp.stack(relative)
    return jnp.roll(stacked, me, axis=0)


def ring_reduce_scatter(parts, exact, axis):
    n = lax.axis_size(axis)
    me = lax.axis_index(axis)
    rows, columns = parts.shape[1], parts.shape[2]
    pad = 16 - 2
    forward_steps = n // 2
    backward_steps = n - 1 - forward_steps

    def pick(stack, offset):
        return lax.dynamic_index_in_dim(stack, (me + offset) % n, 0, keepdims=False)

    def own(offset):
        return pick(parts, offset).astype(jnp.float32), pick(exact, offset)

    def wire(values):
        main, extra = values
        high = extra.astype(jnp.bfloat16)
        low = (extra - high.astype(jnp.float32)).astype(jnp.bfloat16)
        return jnp.concatenate(
            [main.astype(jnp.bfloat16), high[None], low[None], jnp.zeros((pad, columns), jnp.bfloat16)]
        )

    def unwire(packet):
        main = packet[:rows].astype(jnp.float32)
        extra = packet[rows].astype(jnp.float32) + packet[rows + 1].astype(jnp.float32)
        return main, extra

    def add(packet, offset):
        main, extra = unwire(packet)
        own_main, own_extra = own(offset)
        return main + own_main, extra + own_extra

    forward = wire(own(forward_steps))
    backward = wire(own(n - backward_steps))
    for step in range(forward_steps):
        received = shift(forward, axis, 1)
        if step < forward_steps - 1:
            received = lax.optimization_barrier((received, backward))[0]
            forward = wire(add(received, forward_steps - 1 - step))
        else:
            forward = received
        if step < backward_steps:
            received = shift(backward, axis, -1)
            received = lax.optimization_barrier((received, forward))[0]
            if step < backward_steps - 1:
                backward = wire(add(received, n - backward_steps + 1 + step))
            else:
                backward = received
    own_main, own_extra = own(0)
    forward_main, forward_extra = unwire(forward)
    backward_main, backward_extra = unwire(backward)
    return own_main + forward_main + backward_main, own_extra + forward_extra + backward_extra


def token_mask(key_lists, length):
    blocks = key_lists.shape[0]
    columns = jnp.arange(blocks, dtype=jnp.int32)
    block_table = jnp.any(key_lists[:, :, None] == columns[None, None, :], axis=1).astype(
        jnp.float32
    )
    owner = (jnp.arange(length, dtype=jnp.int32) // (length // blocks))[:, None] == columns[None, :]
    one_hot = owner.astype(jnp.float32)
    return jnp.dot(jnp.dot(one_hot, block_table), one_hot.T) > 0.5


def local(
    lower_out,
    upper_out,
    lower_grad,
    upper_grad,
    norm_gain,
    query_weight,
    key_weight,
    value_projection,
    output_weight,
    key_lists,
):
    n_mp = lax.axis_size("mp")
    share = upper_out.shape[3]
    gathered = ring_gather(jnp.stack([upper_out[0, 0], lower_grad[0, 0]]), "mp")
    length = gathered.shape[2]
    whole_upper = jnp.transpose(gathered[:, 0], (1, 0, 2)).reshape(length, n_mp * share)
    whole_grad = jnp.transpose(gathered[:, 1], (1, 0, 2)).reshape(length, n_mp * share)
    stream = whole_upper.astype(jnp.float32)
    inverse = lax.rsqrt(jnp.mean(stream * stream, axis=1, keepdims=True) + 1e-06)
    unit_rows = stream * inverse
    gain_rows = norm_gain[0].astype(jnp.float32)
    normed = (unit_rows * gain_rows).astype(jnp.bfloat16)
    w_query = query_weight[0]
    w_key = key_weight[0]
    w_value = value_projection[0]
    w_output = output_weight[0]
    kv_heads = w_key.shape[1] // HEAD_SIZE
    group_width = w_query.shape[1] // HEAD_SIZE // kv_heads
    query_head_split = jnp.dot(normed, w_query, preferred_element_type=jnp.float32).astype(
        jnp.bfloat16
    )
    query_head_split = query_head_split.reshape(length, kv_heads, group_width, HEAD_SIZE)
    key_head_split = (
        jnp.dot(normed, w_key, preferred_element_type=jnp.float32)
        .astype(jnp.bfloat16)
        .reshape(length, kv_heads, HEAD_SIZE)
    )
    value_head_split = (
        jnp.dot(normed, w_value, preferred_element_type=jnp.float32)
        .astype(jnp.bfloat16)
        .reshape(length, kv_heads, HEAD_SIZE)
    )
    allowed = token_mask(key_lists, length)
    raw_scores = jnp.einsum(
        "qjgd,kjd->jgqk", query_head_split, key_head_split, preferred_element_type=jnp.float32
    ) / math.sqrt(HEAD_SIZE)
    masked = jnp.where(allowed, raw_scores, -1e30)
    row_max = jnp.max(masked, axis=3, keepdims=True)
    exponent = jnp.where(allowed, jnp.exp(masked - row_max), 0.0)
    row_total = jnp.sum(exponent, axis=3, keepdims=True)
    probs_full = exponent / row_total
    probability_half = probs_full.astype(jnp.bfloat16)
    attended = jnp.einsum(
        "jgqk,kjd->qjgd", probability_half, value_head_split, preferred_element_type=jnp.float32
    )
    attended = attended.astype(jnp.bfloat16).reshape(length, -1)
    out_parts = jnp.einsum(
        "lc,cmf->mlf",
        attended,
        w_output.reshape(w_output.shape[0], n_mp, share),
        preferred_element_type=jnp.float32,
    ).astype(jnp.bfloat16)
    attention_gradient = jnp.dot(whole_grad, w_output.T, preferred_element_type=jnp.float32).astype(
        jnp.bfloat16
    )
    attention_gradient = attention_gradient.reshape(length, kv_heads, group_width, HEAD_SIZE)
    prob_grad = jnp.einsum(
        "qjgd,kjd->jgqk", attention_gradient, value_head_split, preferred_element_type=jnp.float32
    )
    score_gradient = (
        probs_full
        * (prob_grad - jnp.sum(prob_grad * probs_full, axis=3, keepdims=True))
        / math.sqrt(HEAD_SIZE)
    )
    score_gradient = score_gradient.astype(jnp.bfloat16)
    value_gradient = jnp.einsum(
        "munr,nmuy->rmy", probability_half, attention_gradient, preferred_element_type=jnp.float32
    )
    value_gradient = value_gradient.astype(jnp.bfloat16).reshape(length, -1)
    query_grad = jnp.einsum(
        "jgqk,kjd->qjgd", score_gradient, key_head_split, preferred_element_type=jnp.float32
    )
    query_grad = query_grad.astype(jnp.bfloat16).reshape(length, -1)
    key_gradient = jnp.einsum(
        "munr,nmuy->rmy", score_gradient, query_head_split, preferred_element_type=jnp.float32
    )
    key_gradient = key_gradient.astype(jnp.bfloat16).reshape(length, -1)
    normed_grad = jnp.dot(query_grad, w_query.T, preferred_element_type=jnp.float32)
    normed_grad = normed_grad + jnp.dot(key_gradient, w_key.T, preferred_element_type=jnp.float32)
    normed_grad = normed_grad + jnp.dot(
        value_gradient, w_value.T, preferred_element_type=jnp.float32
    )
    weighted = gain_rows * normed_grad
    row_stat = jnp.mean(unit_rows * weighted, axis=1, keepdims=True)
    grad_parts = ((weighted - unit_rows * row_stat) * inverse).astype(jnp.bfloat16)
    grad_parts = jnp.transpose(grad_parts.reshape(length, n_mp, share), (1, 0, 2))
    gain_parts = jnp.sum(normed_grad * unit_rows, axis=0).reshape(n_mp, share)
    shares, gain_share = ring_reduce_scatter(
        jnp.concatenate([out_parts, grad_parts], axis=1), gain_parts, "mp"
    )
    out_share, grad_share = shares[:length], shares[length:]
    rebuilt = (lower_out[0, 0].astype(jnp.float32) - out_share).astype(jnp.bfloat16)
    lower_rows = upper_grad[0, 0].astype(jnp.float32) + grad_share
    gain_grad = gain_share + shift(gain_share, "dp", 1)
    entering = lower_rows.astype(jnp.bfloat16)
    sent = from_behind(jnp.stack([rebuilt, entering]), "section", -1)
    return (sent[0][None, None], sent[1][None, None], gain_grad[None])


def solution(mesh):
    placed = (
        P("section", "dp", None, "mp"),
        P("section", "dp", None, "mp"),
        P("section", "dp", None, "mp"),
        P("section", "dp", None, "mp"),
        P("section", None),
        P("section", None, "mp"),
        P("section", None, "mp"),
        P("section", None, "mp"),
        P("section", "mp", None),
        P(),
    )
    return jax.shard_map(
        local,
        mesh=mesh,
        in_specs=placed,
        out_specs=(
            P("section", "dp", None, "mp"),
            P("section", "dp", None, "mp"),
            P("section", "mp"),
        ),
        check_vma=False,
    )
```

```python
import math

import jax
import jax.numpy as jnp
from jax import lax
from jax.sharding import PartitionSpec as P

HEAD_SIZE = 128


def from_behind(x, axis, by):
    length = lax.axis_size(axis)
    pairs = [(i, i + by) for i in range(length) if 0 <= i + by < length]
    return lax.ppermute(x, axis, pairs)


def shift(x, axis, by):
    length = lax.axis_size(axis)
    return lax.ppermute(x, axis, [(i, (i + by) % length) for i in range(length)])


def ring_gather(chunk, axis):
    n = lax.axis_size(axis)
    me = lax.axis_index(axis)
    forward_steps = n // 2
    backward_steps = n - 1 - forward_steps
    relative = [None] * n
    relative[0] = chunk
    forward = chunk
    backward = chunk
    for step in range(forward_steps):
        forward = shift(forward, axis, 1)
        relative[n - 1 - step] = forward
        if step < backward_steps:
            backward = shift(backward, axis, -1)
            relative[step + 1] = backward
    stacked = jnp.stack(relative)
    return jnp.roll(stacked, me, axis=0)


def ring_reduce_scatter(parts, exact, axis):
    n = lax.axis_size(axis)
    me = lax.axis_index(axis)
    rows, columns = parts.shape[1], parts.shape[2]
    pad = 16 - 2
    forward_steps = n // 2
    backward_steps = n - 1 - forward_steps

    parts = jnp.roll(parts, -me, axis=0)
    exact = jnp.roll(exact, -me, axis=0)

    def pick(stack, offset):
        return stack[offset % n]

    def own(offset):
        return pick(parts, offset).astype(jnp.float32), pick(exact, offset)

    def wire(values):
        main, extra = values
        high = extra.astype(jnp.bfloat16)
        low = (extra - high.astype(jnp.float32)).astype(jnp.bfloat16)
        return jnp.concatenate(
            [main.astype(jnp.bfloat16), high[None], low[None], jnp.zeros((pad, columns), jnp.bfloat16)]
        )

    def unwire(packet):
        main = packet[:rows].astype(jnp.float32)
        extra = packet[rows].astype(jnp.float32) + packet[rows + 1].astype(jnp.float32)
        return main, extra

    def add(packet, offset):
        main, extra = unwire(packet)
        own_main, own_extra = own(offset)
        return main + own_main, extra + own_extra

    forward = wire(own(forward_steps))
    backward = wire(own(n - backward_steps))
    for step in range(forward_steps):
        received = shift(forward, axis, 1)
        if step < forward_steps - 1:
            received = lax.optimization_barrier((received, backward))[0]
            forward = wire(add(received, forward_steps - 1 - step))
        else:
            forward = received
        if step < backward_steps:
            received = shift(backward, axis, -1)
            received = lax.optimization_barrier((received, forward))[0]
            if step < backward_steps - 1:
                backward = wire(add(received, n - backward_steps + 1 + step))
            else:
                backward = received
    own_main, own_extra = own(0)
    forward_main, forward_extra = unwire(forward)
    backward_main, backward_extra = unwire(backward)
    return own_main + forward_main + backward_main, own_extra + forward_extra + backward_extra


def token_mask(key_lists, length):
    blocks = key_lists.shape[0]
    columns = jnp.arange(blocks, dtype=jnp.int32)
    block_table = jnp.any(key_lists[:, :, None] == columns[None, None, :], axis=1).astype(
        jnp.float32
    )
    owner = (jnp.arange(length, dtype=jnp.int32) // (length // blocks))[:, None] == columns[None, :]
    one_hot = owner.astype(jnp.float32)
    return jnp.dot(jnp.dot(one_hot, block_table), one_hot.T) > 0.5


def local(
    lower_out,
    upper_out,
    lower_grad,
    upper_grad,
    norm_gain,
    query_weight,
    key_weight,
    value_projection,
    output_weight,
    key_lists,
):
    n_mp = lax.axis_size("mp")
    share = upper_out.shape[3]
    gathered = ring_gather(jnp.stack([upper_out[0, 0], lower_grad[0, 0]]), "mp")
    length = gathered.shape[2]
    whole_upper = jnp.transpose(gathered[:, 0], (1, 0, 2)).reshape(length, n_mp * share)
    whole_grad = jnp.transpose(gathered[:, 1], (1, 0, 2)).reshape(length, n_mp * share)
    stream = whole_upper.astype(jnp.float32)
    inverse = lax.rsqrt(jnp.mean(stream * stream, axis=1, keepdims=True) + 1e-06)
    unit_rows = stream * inverse
    gain_rows = norm_gain[0].astype(jnp.float32)
    normed = (unit_rows * gain_rows).astype(jnp.bfloat16)
    w_query = query_weight[0]
    w_key = key_weight[0]
    w_value = value_projection[0]
    w_output = output_weight[0]
    kv_heads = w_key.shape[1] // HEAD_SIZE
    group_width = w_query.shape[1] // HEAD_SIZE // kv_heads
    query_head_split = jnp.dot(normed, w_query, preferred_element_type=jnp.float32).astype(
        jnp.bfloat16
    )
    query_head_split = query_head_split.reshape(length, kv_heads, group_width, HEAD_SIZE)
    key_head_split = (
        jnp.dot(normed, w_key, preferred_element_type=jnp.float32)
        .astype(jnp.bfloat16)
        .reshape(length, kv_heads, HEAD_SIZE)
    )
    value_head_split = (
        jnp.dot(normed, w_value, preferred_element_type=jnp.float32)
        .astype(jnp.bfloat16)
        .reshape(length, kv_heads, HEAD_SIZE)
    )
    allowed = token_mask(key_lists, length)
    raw_scores = jnp.einsum(
        "qjgd,kjd->jgqk", query_head_split, key_head_split, preferred_element_type=jnp.float32
    ) / math.sqrt(HEAD_SIZE)
    masked = jnp.where(allowed, raw_scores, -1e30)
    row_max = jnp.max(masked, axis=3, keepdims=True)
    exponent = jnp.where(allowed, jnp.exp(masked - row_max), 0.0)
    row_total = jnp.sum(exponent, axis=3, keepdims=True)
    probs_full = exponent / row_total
    probability_half = probs_full.astype(jnp.bfloat16)
    attended = jnp.einsum(
        "jgqk,kjd->qjgd", probability_half, value_head_split, preferred_element_type=jnp.float32
    )
    attended = attended.astype(jnp.bfloat16).reshape(length, -1)
    out_parts = jnp.einsum(
        "lc,cmf->mlf",
        attended,
        w_output.reshape(w_output.shape[0], n_mp, share),
        preferred_element_type=jnp.float32,
    ).astype(jnp.bfloat16)
    attention_gradient = jnp.dot(whole_grad, w_output.T, preferred_element_type=jnp.float32).astype(
        jnp.bfloat16
    )
    attention_gradient = attention_gradient.reshape(length, kv_heads, group_width, HEAD_SIZE)
    prob_grad = jnp.einsum(
        "qjgd,kjd->jgqk", attention_gradient, value_head_split, preferred_element_type=jnp.float32
    )
    score_gradient = (
        probs_full
        * (prob_grad - jnp.sum(prob_grad * probs_full, axis=3, keepdims=True))
        / math.sqrt(HEAD_SIZE)
    )
    score_gradient = score_gradient.astype(jnp.bfloat16)
    value_gradient = jnp.einsum(
        "munr,nmuy->rmy", probability_half, attention_gradient, preferred_element_type=jnp.float32
    )
    value_gradient = value_gradient.astype(jnp.bfloat16).reshape(length, -1)
    query_grad = jnp.einsum(
        "jgqk,kjd->qjgd", score_gradient, key_head_split, preferred_element_type=jnp.float32
    )
    query_grad = query_grad.astype(jnp.bfloat16).reshape(length, -1)
    key_gradient = jnp.einsum(
        "munr,nmuy->rmy", score_gradient, query_head_split, preferred_element_type=jnp.float32
    )
    key_gradient = key_gradient.astype(jnp.bfloat16).reshape(length, -1)
    normed_grad = jnp.dot(query_grad, w_query.T, preferred_element_type=jnp.float32)
    normed_grad = normed_grad + jnp.dot(key_gradient, w_key.T, preferred_element_type=jnp.float32)
    normed_grad = normed_grad + jnp.dot(
        value_gradient, w_value.T, preferred_element_type=jnp.float32
    )
    weighted = gain_rows * normed_grad
    row_stat = jnp.mean(unit_rows * weighted, axis=1, keepdims=True)
    grad_parts = ((weighted - unit_rows * row_stat) * inverse).astype(jnp.bfloat16)
    grad_parts = jnp.transpose(grad_parts.reshape(length, n_mp, share), (1, 0, 2))
    gain_parts = jnp.sum(normed_grad * unit_rows, axis=0).reshape(n_mp, share)
    gain_parts = gain_parts + shift(gain_parts, "dp", 1)
    shares, gain_share = ring_reduce_scatter(
        jnp.concatenate([out_parts, grad_parts], axis=1), gain_parts, "mp"
    )
    out_share, grad_share = shares[:length], shares[length:]
    rebuilt = (lower_out[0, 0].astype(jnp.float32) - out_share).astype(jnp.bfloat16)
    lower_rows = upper_grad[0, 0].astype(jnp.float32) + grad_share
    gain_grad = gain_share
    entering = lower_rows.astype(jnp.bfloat16)
    sent = from_behind(jnp.stack([rebuilt, entering]), "section", -1)
    return (sent[0][None, None], sent[1][None, None], gain_grad[None])


def solution(mesh):
    placed = (
        P("section", "dp", None, "mp"),
        P("section", "dp", None, "mp"),
        P("section", "dp", None, "mp"),
        P("section", "dp", None, "mp"),
        P("section", None),
        P("section", None, "mp"),
        P("section", None, "mp"),
        P("section", None, "mp"),
        P("section", "mp", None),
        P(),
    )
    return jax.shard_map(
        local,
        mesh=mesh,
        in_specs=placed,
        out_specs=(
            P("section", "dp", None, "mp"),
            P("section", "dp", None, "mp"),
            P("section", "mp"),
        ),
        check_vma=False,
    )
```

```python
import math

import jax
import jax.numpy as jnp
from jax import lax
from jax.sharding import PartitionSpec as P

HEAD_SIZE = 128


def from_behind(x, axis, by):
    length = lax.axis_size(axis)
    pairs = [(i, i + by) for i in range(length) if 0 <= i + by < length]
    return lax.ppermute(x, axis, pairs)


def shift(x, axis, by):
    length = lax.axis_size(axis)
    return lax.ppermute(x, axis, [(i, (i + by) % length) for i in range(length)])


def ring_gather(chunk, axis):
    n = lax.axis_size(axis)
    me = lax.axis_index(axis)
    forward_steps = n // 2
    backward_steps = n - 1 - forward_steps
    relative = [None] * n
    relative[0] = chunk
    forward = chunk
    backward = chunk
    for step in range(forward_steps):
        forward = shift(forward, axis, 1)
        relative[n - 1 - step] = forward
        if step < backward_steps:
            backward = shift(backward, axis, -1)
            relative[step + 1] = backward
    stacked = jnp.stack(relative)
    return jnp.roll(stacked, me, axis=0)


def ring_reduce_scatter(parts, exact, axis):
    n = lax.axis_size(axis)
    me = lax.axis_index(axis)
    rows, columns = parts.shape[1], parts.shape[2]
    pad = 16 - 2
    forward_steps = n // 2
    backward_steps = n - 1 - forward_steps

    def pick(stack, offset):
        return lax.dynamic_index_in_dim(stack, (me + offset) % n, 0, keepdims=False)

    def own(offset):
        return pick(parts, offset).astype(jnp.float32), pick(exact, offset)

    def wire(values):
        main, extra = values
        high = extra.astype(jnp.bfloat16)
        low = (extra - high.astype(jnp.float32)).astype(jnp.bfloat16)
        return jnp.concatenate(
            [main.astype(jnp.bfloat16), high[None], low[None], jnp.zeros((pad, columns), jnp.bfloat16)]
        )

    def unwire(packet):
        main = packet[:rows].astype(jnp.float32)
        extra = packet[rows].astype(jnp.float32) + packet[rows + 1].astype(jnp.float32)
        return main, extra

    def add(packet, offset):
        main, extra = unwire(packet)
        own_main, own_extra = own(offset)
        return main + own_main, extra + own_extra

    forward = wire(own(forward_steps))
    backward = wire(own(n - backward_steps))
    for step in range(forward_steps):
        received = shift(forward, axis, 1)
        if step < forward_steps - 1:
            received = lax.optimization_barrier((received, backward))[0]
            forward = wire(add(received, forward_steps - 1 - step))
        else:
            forward = received
        if step < backward_steps:
            received = shift(backward, axis, -1)
            received = lax.optimization_barrier((received, forward))[0]
            if step < backward_steps - 1:
                backward = wire(add(received, n - backward_steps + 1 + step))
            else:
                backward = received
    own_main, own_extra = own(0)
    forward_main, forward_extra = unwire(forward)
    backward_main, backward_extra = unwire(backward)
    return own_main + forward_main + backward_main, own_extra + forward_extra + backward_extra


def token_mask(key_lists, length):
    blocks = key_lists.shape[0]
    columns = jnp.arange(blocks, dtype=jnp.int32)
    block_table = jnp.any(key_lists[:, :, None] == columns[None, None, :], axis=1).astype(
        jnp.float32
    )
    owner = (jnp.arange(length, dtype=jnp.int32) // (length // blocks))[:, None] == columns[None, :]
    one_hot = owner.astype(jnp.float32)
    return jnp.dot(jnp.dot(one_hot, block_table), one_hot.T) > 0.5


def local(
    lower_out,
    upper_out,
    lower_grad,
    upper_grad,
    norm_gain,
    query_weight,
    key_weight,
    value_projection,
    output_weight,
    key_lists,
):
    n_mp = lax.axis_size("mp")
    share = upper_out.shape[3]
    gathered = ring_gather(jnp.stack([upper_out[0, 0], lower_grad[0, 0]]), "mp")
    length = gathered.shape[2]
    whole_upper = jnp.transpose(gathered[:, 0], (1, 0, 2)).reshape(length, n_mp * share)
    whole_grad = jnp.transpose(gathered[:, 1], (1, 0, 2)).reshape(length, n_mp * share)
    stream = whole_upper.astype(jnp.float32)
    inverse = lax.rsqrt(jnp.mean(stream * stream, axis=1, keepdims=True) + 1e-06)
    unit_rows = stream * inverse
    gain_rows = norm_gain[0].astype(jnp.float32)
    normed = (unit_rows * gain_rows).astype(jnp.bfloat16)
    w_query = query_weight[0]
    w_key = key_weight[0]
    w_value = value_projection[0]
    w_output = output_weight[0]
    kv_heads = w_key.shape[1] // HEAD_SIZE
    group_width = w_query.shape[1] // HEAD_SIZE // kv_heads
    query_head_split = jnp.dot(normed, w_query, preferred_element_type=jnp.float32).astype(
        jnp.bfloat16
    )
    query_head_split = query_head_split.reshape(length, kv_heads, group_width, HEAD_SIZE)
    key_head_split = (
        jnp.dot(normed, w_key, preferred_element_type=jnp.float32)
        .astype(jnp.bfloat16)
        .reshape(length, kv_heads, HEAD_SIZE)
    )
    value_head_split = (
        jnp.dot(normed, w_value, preferred_element_type=jnp.float32)
        .astype(jnp.bfloat16)
        .reshape(length, kv_heads, HEAD_SIZE)
    )
    allowed = token_mask(key_lists, length)
    raw_scores = jnp.einsum(
        "qjgd,kjd->jgqk", query_head_split, key_head_split, preferred_element_type=jnp.float32
    ) / math.sqrt(HEAD_SIZE)
    masked = jnp.where(allowed, raw_scores, -1e30)
    row_max = jnp.max(masked, axis=3, keepdims=True)
    exponent = jnp.where(allowed, jnp.exp(masked - row_max), 0.0)
    row_total = jnp.sum(exponent, axis=3, keepdims=True)
    probs_full = exponent / row_total
    probability_half = probs_full.astype(jnp.bfloat16)
    attended = jnp.einsum(
        "jgqk,kjd->qjgd", probability_half, value_head_split, preferred_element_type=jnp.float32
    )
    attended = attended.astype(jnp.bfloat16).reshape(length, -1)
    out_parts = jnp.einsum(
        "lc,mcf->mlf",
        attended,
        jnp.transpose(w_output.reshape(w_output.shape[0], n_mp, share), (1, 0, 2)),
        preferred_element_type=jnp.float32,
    ).astype(jnp.bfloat16)
    attention_gradient = jnp.dot(whole_grad, w_output.T, preferred_element_type=jnp.float32).astype(
        jnp.bfloat16
    )
    attention_gradient = attention_gradient.reshape(length, kv_heads, group_width, HEAD_SIZE)
    prob_grad = jnp.einsum(
        "qjgd,kjd->jgqk", attention_gradient, value_head_split, preferred_element_type=jnp.float32
    )
    score_gradient = (
        probs_full
        * (prob_grad - jnp.sum(prob_grad * probs_full, axis=3, keepdims=True))
        / math.sqrt(HEAD_SIZE)
    )
    score_gradient = score_gradient.astype(jnp.bfloat16)
    value_gradient = jnp.einsum(
        "munr,nmuy->rmy", probability_half, attention_gradient, preferred_element_type=jnp.float32
    )
    value_gradient = value_gradient.astype(jnp.bfloat16).reshape(length, -1)
    query_grad = jnp.einsum(
        "jgqk,kjd->qjgd", score_gradient, key_head_split, preferred_element_type=jnp.float32
    )
    query_grad = query_grad.astype(jnp.bfloat16).reshape(length, -1)
    key_gradient = jnp.einsum(
        "munr,nmuy->rmy", score_gradient, query_head_split, preferred_element_type=jnp.float32
    )
    key_gradient = key_gradient.astype(jnp.bfloat16).reshape(length, -1)
    unit_chunks = gathered[:, 0].astype(jnp.float32) * inverse.reshape(1, length, 1)
    gain_chunks = gain_rows.reshape(n_mp, 1, share)
    normed_grad = jnp.einsum(
        "th,mfh->mtf", query_grad, w_query.reshape(n_mp, share, -1), preferred_element_type=jnp.float32
    )
    normed_grad = normed_grad + jnp.einsum(
        "th,mfh->mtf", key_gradient, w_key.reshape(n_mp, share, -1), preferred_element_type=jnp.float32
    )
    normed_grad = normed_grad + jnp.einsum(
        "th,mfh->mtf", value_gradient, w_value.reshape(n_mp, share, -1), preferred_element_type=jnp.float32
    )
    weighted = gain_chunks * normed_grad
    row_stat = jnp.sum(unit_chunks * weighted, axis=(0, 2), keepdims=True) / (n_mp * share)
    grad_parts = ((weighted - unit_chunks * row_stat) * inverse.reshape(1, length, 1)).astype(
        jnp.bfloat16
    )
    gain_parts = jnp.sum(normed_grad * unit_chunks, axis=1)
    shares, gain_share = ring_reduce_scatter(
        jnp.concatenate([out_parts, grad_parts], axis=1), gain_parts, "mp"
    )
    out_share, grad_share = shares[:length], shares[length:]
    rebuilt = (lower_out[0, 0].astype(jnp.float32) - out_share).astype(jnp.bfloat16)
    lower_rows = upper_grad[0, 0].astype(jnp.float32) + grad_share
    gain_grad = gain_share + shift(gain_share, "dp", 1)
    entering = lower_rows.astype(jnp.bfloat16)
    sent = from_behind(jnp.stack([rebuilt, entering]), "section", -1)
    return (sent[0][None, None], sent[1][None, None], gain_grad[None])


def solution(mesh):
    placed = (
        P("section", "dp", None, "mp"),
        P("section", "dp", None, "mp"),
        P("section", "dp", None, "mp"),
        P("section", "dp", None, "mp"),
        P("section", None),
        P("section", None, "mp"),
        P("section", None, "mp"),
        P("section", None, "mp"),
        P("section", "mp", None),
        P(),
    )
    return jax.shard_map(
        local,
        mesh=mesh,
        in_specs=placed,
        out_specs=(
            P("section", "dp", None, "mp"),
            P("section", "dp", None, "mp"),
            P("section", "mp"),
        ),
        check_vma=False,
    )
```

```python
import math

import jax
import jax.numpy as jnp
from jax import lax
from jax.sharding import PartitionSpec as P

HEAD_SIZE = 128


def from_behind(x, axis, by):
    length = lax.axis_size(axis)
    pairs = [(i, i + by) for i in range(length) if 0 <= i + by < length]
    return lax.ppermute(x, axis, pairs)


def shift(x, axis, by):
    length = lax.axis_size(axis)
    return lax.ppermute(x, axis, [(i, (i + by) % length) for i in range(length)])


def ring_gather(chunk, axis):
    n = lax.axis_size(axis)
    me = lax.axis_index(axis)
    forward_steps = n // 2
    backward_steps = n - 1 - forward_steps
    relative = [None] * n
    relative[0] = chunk
    forward = chunk
    backward = chunk
    for step in range(forward_steps):
        forward = shift(forward, axis, 1)
        relative[n - 1 - step] = forward
        if step < backward_steps:
            backward = shift(backward, axis, -1)
            relative[step + 1] = backward
    stacked = jnp.stack(relative)
    return jnp.roll(stacked, me, axis=0)


def ring_reduce_scatter(parts, exact, axis):
    n = lax.axis_size(axis)
    me = lax.axis_index(axis)
    rows, columns = parts.shape[1], parts.shape[2]
    pad = 16 - 2
    forward_steps = n // 2
    backward_steps = n - 1 - forward_steps

    def pick(stack, offset):
        return lax.dynamic_index_in_dim(stack, (me + offset) % n, 0, keepdims=False)

    def own(offset):
        return pick(parts, offset).astype(jnp.float32), pick(exact, offset)

    def wire(values):
        main, extra = values
        high = extra.astype(jnp.bfloat16)
        low = (extra - high.astype(jnp.float32)).astype(jnp.bfloat16)
        return jnp.concatenate(
            [main.astype(jnp.bfloat16), high[None], low[None], jnp.zeros((pad, columns), jnp.bfloat16)]
        )

    def unwire(packet):
        main = packet[:rows].astype(jnp.float32)
        extra = packet[rows].astype(jnp.float32) + packet[rows + 1].astype(jnp.float32)
        return main, extra

    def add(packet, offset):
        main, extra = unwire(packet)
        own_main, own_extra = own(offset)
        return main + own_main, extra + own_extra

    forward = wire(own(forward_steps))
    backward = wire(own(n - backward_steps))
    for step in range(forward_steps):
        received = shift(forward, axis, 1)
        if step < forward_steps - 1:
            received = lax.optimization_barrier((received, backward))[0]
            forward = wire(add(received, forward_steps - 1 - step))
        else:
            forward = received
        if step < backward_steps:
            received = shift(backward, axis, -1)
            received = lax.optimization_barrier((received, forward))[0]
            if step < backward_steps - 1:
                backward = wire(add(received, n - backward_steps + 1 + step))
            else:
                backward = received
    own_main, own_extra = own(0)
    forward_main, forward_extra = unwire(forward)
    backward_main, backward_extra = unwire(backward)
    return own_main + forward_main + backward_main, own_extra + forward_extra + backward_extra


def token_mask(key_lists, length):
    blocks = key_lists.shape[0]
    columns = jnp.arange(blocks, dtype=jnp.int32)
    block_table = jnp.any(key_lists[:, :, None] == columns[None, None, :], axis=1).astype(
        jnp.float32
    )
    owner = (jnp.arange(length, dtype=jnp.int32) // (length // blocks))[:, None] == columns[None, :]
    one_hot = owner.astype(jnp.float32)
    return jnp.dot(jnp.dot(one_hot, block_table), one_hot.T) > 0.5


def local(
    lower_out,
    upper_out,
    lower_grad,
    upper_grad,
    norm_gain,
    query_weight,
    key_weight,
    value_projection,
    output_weight,
    key_lists,
):
    n_mp = lax.axis_size("mp")
    share = upper_out.shape[3]
    gathered = ring_gather(jnp.stack([upper_out[0, 0], lower_grad[0, 0]]), "mp")
    length = gathered.shape[2]
    whole_upper = jnp.transpose(gathered[:, 0], (1, 0, 2)).reshape(length, n_mp * share)
    whole_grad = jnp.transpose(gathered[:, 1], (1, 0, 2)).reshape(length, n_mp * share)
    stream = whole_upper.astype(jnp.float32)
    inverse = lax.rsqrt(jnp.mean(stream * stream, axis=1, keepdims=True) + 1e-06)
    unit_rows = stream * inverse
    gain_rows = norm_gain[0].astype(jnp.float32)
    normed = (unit_rows * gain_rows).astype(jnp.bfloat16)
    w_query = query_weight[0]
    w_key = key_weight[0]
    w_value = value_projection[0]
    w_output = output_weight[0]
    kv_heads = w_key.shape[1] // HEAD_SIZE
    group_width = w_query.shape[1] // HEAD_SIZE // kv_heads
    query_head_split = jnp.dot(normed, w_query, preferred_element_type=jnp.float32).astype(
        jnp.bfloat16
    )
    query_head_split = query_head_split.reshape(length, kv_heads, group_width, HEAD_SIZE)
    key_head_split = (
        jnp.dot(normed, w_key, preferred_element_type=jnp.float32)
        .astype(jnp.bfloat16)
        .reshape(length, kv_heads, HEAD_SIZE)
    )
    value_head_split = (
        jnp.dot(normed, w_value, preferred_element_type=jnp.float32)
        .astype(jnp.bfloat16)
        .reshape(length, kv_heads, HEAD_SIZE)
    )
    allowed = token_mask(key_lists, length)
    raw_scores = jnp.einsum(
        "qjgd,kjd->jgqk", query_head_split, key_head_split, preferred_element_type=jnp.float32
    ) / math.sqrt(HEAD_SIZE)
    masked = jnp.where(allowed, raw_scores, -1e30)
    row_max = jnp.max(masked, axis=3, keepdims=True)
    exponent = jnp.where(allowed, jnp.exp(masked - row_max), 0.0)
    row_total = jnp.sum(exponent, axis=3, keepdims=True)
    probs_full = exponent / row_total
    probability_half = probs_full.astype(jnp.bfloat16)
    attended = jnp.einsum(
        "jgqk,kjd->qjgd", probability_half, value_head_split, preferred_element_type=jnp.float32
    )
    attended = attended.astype(jnp.bfloat16).reshape(length, -1)
    out_parts = jnp.einsum(
        "lc,cmf->mlf",
        attended,
        w_output.reshape(w_output.shape[0], n_mp, share),
        preferred_element_type=jnp.float32,
    ).astype(jnp.bfloat16)
    attention_gradient = jnp.dot(whole_grad, w_output.T, preferred_element_type=jnp.float32).astype(
        jnp.bfloat16
    )
    attention_gradient = attention_gradient.reshape(length, kv_heads, group_width, HEAD_SIZE)
    prob_grad = jnp.einsum(
        "qjgd,kjd->jgqk", attention_gradient, value_head_split, preferred_element_type=jnp.float32
    )
    score_gradient = (
        probs_full
        * (prob_grad - jnp.sum(prob_grad * probs_full, axis=3, keepdims=True))
        / math.sqrt(HEAD_SIZE)
    )
    score_gradient = score_gradient.astype(jnp.bfloat16)
    value_gradient = jnp.einsum(
        "munr,nmuy->rmy", probability_half, attention_gradient, preferred_element_type=jnp.float32
    )
    value_gradient = value_gradient.astype(jnp.bfloat16).reshape(length, -1)
    query_grad = jnp.einsum(
        "jgqk,kjd->qjgd", score_gradient, key_head_split, preferred_element_type=jnp.float32
    )
    query_grad = query_grad.astype(jnp.bfloat16).reshape(length, -1)
    key_gradient = jnp.einsum(
        "munr,nmuy->rmy", score_gradient, query_head_split, preferred_element_type=jnp.float32
    )
    key_gradient = key_gradient.astype(jnp.bfloat16).reshape(length, -1)
    normed_grad = jnp.dot(query_grad, w_query.T, preferred_element_type=jnp.float32)
    normed_grad = normed_grad + jnp.dot(key_gradient, w_key.T, preferred_element_type=jnp.float32)
    normed_grad = normed_grad + jnp.dot(
        value_gradient, w_value.T, preferred_element_type=jnp.float32
    )
    weighted = gain_rows * normed_grad
    row_stat = jnp.mean(unit_rows * weighted, axis=1, keepdims=True)
    grad_parts = ((weighted - unit_rows * row_stat) * inverse).astype(jnp.bfloat16)
    grad_parts = jnp.transpose(grad_parts.reshape(length, n_mp, share), (1, 0, 2))
    gain_parts = jnp.sum(normed_grad * unit_rows, axis=0).reshape(n_mp, share)
    gain_parts = gain_parts + shift(gain_parts, "dp", 1)
    shares, gain_share = ring_reduce_scatter(
        jnp.concatenate([out_parts, grad_parts], axis=1), gain_parts, "mp"
    )
    out_share, grad_share = shares[:length], shares[length:]
    rebuilt = (lower_out[0, 0].astype(jnp.float32) - out_share).astype(jnp.bfloat16)
    lower_rows = upper_grad[0, 0].astype(jnp.float32) + grad_share
    gain_grad = gain_share
    entering = lower_rows.astype(jnp.bfloat16)
    sent = from_behind(jnp.stack([rebuilt, entering]), "section", -1)
    return (sent[0][None, None], sent[1][None, None], gain_grad[None])


def solution(mesh):
    placed = (
        P("section", "dp", None, "mp"),
        P("section", "dp", None, "mp"),
        P("section", "dp", None, "mp"),
        P("section", "dp", None, "mp"),
        P("section", None),
        P("section", None, "mp"),
        P("section", None, "mp"),
        P("section", None, "mp"),
        P("section", "mp", None),
        P(),
    )
    return jax.shard_map(
        local,
        mesh=mesh,
        in_specs=placed,
        out_specs=(
            P("section", "dp", None, "mp"),
            P("section", "dp", None, "mp"),
            P("section", "mp"),
        ),
        check_vma=False,
    )
```
